32 devices in a mesh: row: 4 (over y, x), col: 4 (over z), layer: 2 (over core).
Axes of the slice: x: 2, y: 2, z: 4, core: 2. Of those that a mesh axis runs over, the one named last changes fastest.
Arguments:
- x_blocks: bfloat16 [64, 64, 4, 256], P('col', None, 'row'), may hold values from -1 to 1
- x_cols: int32 [64, 4, 4], P('col', 'row'), may hold values from 0 to 15, as said below
- x_count: int32 [64, 4], P('col', 'row'), may hold values from 1 to 4, as said below
- out_cols: int32 [64, 4, 8], P('col', 'row'), may hold values from 0 to 15, as said below
Outputs:
- product: float32 [64, 64, 4, 512], P('col', None, 'row', 'layer')
The draws below stay inside these ranges and needn't reach their ends.
Inputs may be any that keep to these rules, and one draw needn't show every extreme that they name: `x_cols`: within one block row and tile the 4 column entries are distinct. For every tile column t, at least one block row R has x_count[R,t] = 4. `out_cols`: within one block row and tile the 8 column entries are distinct.
All inputs are finite; a program needn't handle non-finite values.
Results may differ from the reference program's by a relative error of at most 0.0003.
Values may be sent and summed in bfloat16 or wider, within the bound.
No kernel may reach another device: no remote copies, remote signals or barrier semaphores. Data moves between devices by JAX's collectives and lax.ppermute only.
A program may use at most 64 MiB of HBM per device.

```python
import jax
import jax.numpy as jnp
from jax import lax

BS = 64
RB = 16
S = 4
SO = 8
TILES = 4
NB = 64


def distinct_prefix(key, width):
    base = jnp.broadcast_to(jnp.arange(RB, dtype=jnp.int32), (NB, TILES, RB))
    shuffled = jax.random.permutation(key, base, axis=2, independent=True)
    return shuffled[:, :, :width]


def draw_x_cols(key, part):
    return distinct_prefix(jax.random.fold_in(key, 11), S)


def draw_out_cols(key, part):
    return distinct_prefix(jax.random.fold_in(key, 23), SO)


def draw_x_count(key, part):
    first, second, third = jax.random.split(jax.random.fold_in(key, 37), 3)
    base = jax.random.randint(first, (NB, TILES), 1, S + 1, dtype=jnp.int32)
    extra = jax.random.randint(second, (NB, 1), 0, S, dtype=jnp.int32)
    counts = jnp.minimum(base + extra, S)
    picked = jax.random.randint(third, (1, TILES), 0, NB, dtype=jnp.int32)
    row_ids = jnp.arange(NB, dtype=jnp.int32)[:, None]
    return jnp.where(row_ids == picked, S, counts).astype(jnp.int32)


def steps_of(key, extent, cuts, smallest, high):
    level = 1.0
    for axis_at, shards_of in cuts:
        steps = jax.random.uniform(jax.random.fold_in(jax.random.fold_in(key, 6), axis_at), (shards_of,), jnp.float32, smallest / len(cuts), high / len(cuts))
        level = level * jnp.repeat(jnp.exp(steps), extent[axis_at] // shards_of).reshape((-1,) + (1,) * (len(extent) - 1 - axis_at))
    return level


def bell_draw(rng, extent, spread, limit, pieces=(), kind=jnp.bfloat16):
    array = spread * jax.random.normal(rng, extent, jnp.float32)
    if pieces:
        array = array * steps_of(rng, extent, pieces, -0.22, 0.18)
    return jnp.clip(array, -limit, limit).astype(kind)


def setup_inputs(seed: int = 0) -> dict:
    streams_of = jax.random.split(jax.random.key(seed), 5)
    return {
        "x_blocks": bell_draw(streams_of[0], (NB, BS, TILES, S * BS), 0.17, 1.0, ((0, 4), (2, 4))),
        "x_cols": draw_x_cols(jax.random.fold_in(streams_of[4], 71), 0),
        "x_count": draw_x_count(jax.random.fold_in(streams_of[4], 71), 0),
        "out_cols": draw_out_cols(jax.random.fold_in(streams_of[4], 71), 0),
    }


def reference(x_blocks, x_cols, x_count, out_cols):
    lanes = x_blocks.shape[3]
    slot_of_lane = jnp.arange(lanes, dtype=jnp.int32) // BS
    keep = slot_of_lane[None, None, None, :] < x_count[:, None, :, None]
    values = jnp.where(keep, x_blocks, jnp.zeros((), x_blocks.dtype))
    tile_base = (jnp.arange(TILES, dtype=jnp.int32) * RB)[:, None]

    def one_row(inputs):
        a_row, a_cols, o_cols = inputs
        source = (tile_base + a_cols).reshape(-1).astype(jnp.int32)
        count_k = source.shape[0]
        b_cols = x_cols[source]
        b_vals = values[source].astype(jnp.float32).reshape(count_k, BS, TILES, S, BS)
        match = (b_cols[:, :, None, :] == o_cols[None, :, :, None]).astype(jnp.float32)
        picked = jnp.einsum('ktoq,kbtqc->ktobc', match, b_vals)
        left = a_row.astype(jnp.float32).reshape(BS, count_k, BS)
        result = jnp.einsum('akb,ktobc->atoc', left, picked)
        return result.reshape(BS, TILES, SO * BS)

    return lax.map(one_row, (values, x_cols, out_cols))
```

```python
import jax
import jax.numpy as jnp
from jax import lax
from jax.sharding import PartitionSpec as P


def spread(values, cols, index_count):
    ids = lax.broadcasted_iota(jnp.int32, (1, index_count, 1), 1)
    hit = cols[:, None, :] == ids
    zero = jnp.zeros((), values.dtype)
    out = jnp.zeros(values.shape[:2] + (index_count, values.shape[3]), values.dtype)
    for s in range(values.shape[2]):
        out = out + jnp.where(hit[:, None, :, s, None], values[:, :, s, None, :], zero)
    return out


def per_device(x_blocks, x_cols, x_count, out_cols):
    row_count, width, _, lanes = x_blocks.shape
    slots = lanes // width
    values = x_blocks[:, :, 0, :]
    slot_of_lane = lax.broadcasted_iota(jnp.int32, (1, 1, lanes), 2) // width
    values = jnp.where(slot_of_lane < x_count[:, :, None], values, jnp.zeros((), values.dtype))
    columns = x_cols[:, 0, :]
    layers = lax.axis_size("layer")
    share = out_cols.shape[2] // layers
    wanted = lax.dynamic_slice_in_dim(out_cols[:, 0, :], lax.axis_index("layer") * share, share, axis=1)

    left_vals = lax.all_gather(values, "row")
    left_cols = lax.all_gather(columns, "row")
    upper_vals = lax.all_gather(values, "col")
    upper_cols = lax.all_gather(columns, "col")
    tiles = left_vals.shape[0]
    per_tile = row_count

    def step(t, total):
        a = left_vals[t].reshape(row_count, width, slots, width)
        a = spread(a, left_cols[t], per_tile)
        b = upper_vals[t].reshape(per_tile, width, slots, width)
        b = spread(b, upper_cols[t], per_tile)
        a = a.reshape(row_count * width, per_tile * width)
        b = b.reshape(per_tile * width, per_tile * width)
        return total + jnp.dot(a, b, preferred_element_type=jnp.float32)

    total = jnp.zeros((row_count * width, per_tile * width), jnp.float32)
    total = lax.fori_loop(0, tiles, step, total)
    total = total.reshape(row_count, width, per_tile, width)
    ids = lax.broadcasted_iota(jnp.int32, (1, 1, 1, per_tile, 1), 3)
    hit = wanted[:, None, :, None, None] == ids
    picked = jnp.where(hit, total[:, :, None, :, :], jnp.zeros((), jnp.float32)).sum(axis=3)
    return picked.reshape(row_count, width, 1, share * width)


def solution(mesh):
    placed = (
        P("col", None, "row", None),
        P("col", "row", None),
        P("col", "row"),
        P("col", "row", None),
    )
    return jax.shard_map(
        per_device,
        mesh=mesh,
        in_specs=placed,
        out_specs=P("col", None, "row", "layer"),
        check_vma=False,
    )
```

```python
import functools

import jax
import jax.numpy as jnp
from jax import lax
from jax.experimental import pallas as pl
from jax.experimental.pallas import tpu as pltpu
from jax.sharding import PartitionSpec as P


def step_kernel(a_cols, b_cols, want, a_ref, b_ref, acc_ref, out_ref, big_ref):
    width = a_ref.shape[1]
    slots = a_ref.shape[2] // width
    outs = want.shape[0] // pl.num_programs(0)
    seg = slots * width
    r = pl.program_id(0)
    chunk = lax.broadcasted_iota(jnp.int32, (width, seg), 1) // width
    zero = jnp.zeros((width, seg), b_ref.dtype)
    for p in range(slots):
        k = a_cols[r * slots + p]
        blk = b_ref[k]
        for o in range(outs):
            j = want[r * outs + o]
            hit = jnp.int32(slots)
            for q in range(slots):
                hit = jnp.where(b_cols[k * slots + q] == j, jnp.int32(q), hit)
            big_ref[p * width:(p + 1) * width, o * seg:(o + 1) * seg] = jnp.where(chunk == hit, blk, zero)
    prod = jnp.dot(a_ref[0], big_ref[...], preferred_element_type=jnp.float32)
    lane = lax.broadcasted_iota(jnp.int32, (width, 2 * width), 1)
    groups = []
    folded = []
    for o in range(outs):
        part = prod[:, o * seg:(o + 1) * seg]
        half = seg // 2
        while half >= width:
            part = part + pltpu.roll(part, half, 1)
            half //= 2
        folded.append(part[:, :2 * width])
    for g in range(outs // 2):
        groups.append(jnp.where(lane < width, folded[2 * g], folded[2 * g + 1]))
    out_ref[0] = acc_ref[0] + jnp.concatenate(groups, axis=1)


def one_step(acc, left, right, a_cols, b_cols, want):
    rows, width, seg = acc.shape[0], left.shape[1], left.shape[2]
    outs = want.shape[0] // rows
    grid_spec = pltpu.PrefetchScalarGridSpec(
        num_scalar_prefetch=3,
        grid=(rows,),
        in_specs=[
            pl.BlockSpec((1, width, seg), lambda r, *_: (r, 0, 0)),
            pl.BlockSpec(right.shape, lambda r, *_: (0, 0, 0)),
            pl.BlockSpec((1, width, acc.shape[2]), lambda r, *_: (r, 0, 0)),
        ],
        out_specs=pl.BlockSpec((1, width, acc.shape[2]), lambda r, *_: (r, 0, 0)),
        scratch_shapes=[pltpu.VMEM((seg, outs * seg), right.dtype)],
    )
    return pl.pallas_call(
        step_kernel,
        grid_spec=grid_spec,
        out_shape=jax.ShapeDtypeStruct(acc.shape, acc.dtype),
        input_output_aliases={5: 0},
    )(a_cols, b_cols, want, left, right, acc)


def per_device(x_blocks, x_cols, x_count, out_cols):
    row_count, width, _, lanes = x_blocks.shape
    slots = lanes // width
    values = x_blocks[:, :, 0, :]
    slot_of_lane = lax.broadcasted_iota(jnp.int32, (1, 1, lanes), 2) // width
    values = jnp.where(slot_of_lane < x_count[:, :, None], values, jnp.zeros((), values.dtype))
    columns = x_cols[:, 0, :].reshape(-1)
    extra = jnp.zeros((1, width, lanes), values.dtype)
    extra = extra.at[0, 0, :columns.shape[0]].set(columns.astype(values.dtype))
    payload = jnp.concatenate([values, extra], axis=0)

    rows_n = lax.axis_size("row")
    cols_n = lax.axis_size("col")
    layers = lax.axis_size("layer")
    steps = rows_n // layers
    me_r = lax.axis_index("row")
    me_c = lax.axis_index("col")
    me_l = lax.axis_index("layer")

    def flat(r, c, l):
        return (r * cols_n + c) * layers + l

    want = out_cols[:, 0, :].reshape(-1)
    outs = out_cols.shape[2]
    total = jnp.zeros((row_count, width, outs * width), jnp.float32)
    for s in range(steps):
        left_pairs = []
        right_pairs = []
        for r in range(rows_n):
            for c in range(cols_n):
                for l in range(layers):
                    t = (r + c + s + l * steps) % rows_n
                    left_pairs.append((flat(t, c, l), flat(r, c, l)))
                    right_pairs.append((flat(r, t, l), flat(r, c, l)))
        left = lax.ppermute(payload, ("row", "col", "layer"), left_pairs)
        right = lax.ppermute(payload, ("row", "col", "layer"), right_pairs)
        a_cols = left[row_count, 0, :columns.shape[0]].astype(jnp.int32)
        b_cols = right[row_count, 0, :columns.shape[0]].astype(jnp.int32)
        total = one_step(total, left, right, a_cols, b_cols, want)

    share = outs // layers * width
    if layers == 2:
        mine = lax.dynamic_slice_in_dim(total, me_l * share, share, axis=2)
        theirs = lax.dynamic_slice_in_dim(total, (1 - me_l) * share, share, axis=2)
        got = lax.ppermute(theirs, "layer", [(0, 1), (1, 0)])
        result = mine + got
    else:
        result = lax.psum_scatter(total, "layer", scatter_dimension=2, tiled=True)
    return result[:, :, None, :]


def solution(mesh):
    placed = (
        P("col", None, "row", None),
        P("col", "row", None),
        P("col", "row"),
        P("col", "row", None),
    )
    return jax.shard_map(
        per_device,
        mesh=mesh,
        in_specs=placed,
        out_specs=P("col", None, "row", "layer"),
        check_vma=False,
    )
```

```python
import functools

import jax
import jax.numpy as jnp
from jax import lax
from jax.experimental import pallas as pl
from jax.experimental.pallas import tpu as pltpu
from jax.sharding import PartitionSpec as P


def step_kernel(a_cols, b_cols, want, a_ref, b_ref, mine_in, theirs_in, mine_ref, theirs_ref, sel_ref):
    width = a_ref.shape[1]
    seg = a_ref.shape[2]
    slots = seg // width
    outs = want.shape[0] // pl.num_programs(0)
    r = pl.program_id(0)
    chunk = lax.broadcasted_iota(jnp.int32, (width, seg), 1) // width
    zero = jnp.zeros((width, seg), b_ref.dtype)
    for p in range(slots):
        k = a_cols[r * slots + p]
        blk = b_ref[k]
        for g in range(outs // slots):
            placed = zero
            for i in range(slots):
                j = want[r * outs + g * slots + i]
                hit = jnp.int32(slots)
                for q in range(slots):
                    hit = jnp.where(b_cols[k * slots + q] == j, jnp.int32(q), hit)
                shift = ((i - hit + slots) % slots) * width
                rolled = pltpu.roll(blk, shift, 1)
                placed = jnp.where(jnp.logical_and(chunk == i, hit < slots), rolled, placed)
            sel_ref[p * width:(p + 1) * width, g * seg:(g + 1) * seg] = placed
    prod = jnp.dot(a_ref[0], sel_ref[...], preferred_element_type=jnp.float32)
    half = prod.shape[1] // 2
    mine_ref[0] = mine_in[0] + prod[:, :half]
    theirs_ref[0] = theirs_in[0] + prod[:, half:]


def one_step(mine, theirs, left, right, a_cols, b_cols, want):
    rows, width, seg = mine.shape[0], left.shape[1], left.shape[2]
    outs = want.shape[0] // rows
    block = pl.BlockSpec((1, width, mine.shape[2]), lambda r, *_: (r, 0, 0))
    grid_spec = pltpu.PrefetchScalarGridSpec(
        num_scalar_prefetch=3,
        grid=(rows,),
        in_specs=[
            pl.BlockSpec((1, width, seg), lambda r, *_: (r, 0, 0)),
            pl.BlockSpec(right.shape, lambda r, *_: (0, 0, 0)),
            block,
            block,
        ],
        out_specs=[block, block],
        scratch_shapes=[pltpu.VMEM((seg, outs * width), right.dtype)],
    )
    cost = pl.CostEstimate(
        flops=2 * rows * width * seg * outs * width,
        transcendentals=0,
        bytes_accessed=2 * (left.size + right.size) + 8 * (mine.size + theirs.size),
    )
    return pl.pallas_call(
        step_kernel,
        grid_spec=grid_spec,
        out_shape=[jax.ShapeDtypeStruct(mine.shape, mine.dtype)] * 2,
        input_output_aliases={5: 0, 6: 1},
        cost_estimate=cost,
    )(a_cols, b_cols, want, left, right, mine, theirs)


def per_device(x_blocks, x_cols, x_count, out_cols):
    row_count, width, _, lanes = x_blocks.shape
    slots = lanes // width
    values = x_blocks[:, :, 0, :]
    slot_of_lane = lax.broadcasted_iota(jnp.int32, (1, 1, lanes), 2) // width
    values = jnp.where(slot_of_lane < x_count[:, :, None], values, jnp.zeros((), values.dtype))
    columns = x_cols[:, 0, :].reshape(-1)
    extra = jnp.zeros((1, width, lanes), values.dtype)
    extra = extra.at[0, 0, :columns.shape[0]].set(columns.astype(values.dtype))
    payload = jnp.concatenate([values, extra], axis=0)

    rows_n = lax.axis_size("row")
    cols_n = lax.axis_size("col")
    layers = lax.axis_size("layer")
    steps = rows_n // layers
    me_r = lax.axis_index("row")
    me_c = lax.axis_index("col")
    me_l = lax.axis_index("layer")

    def flat(r, c, l):
        return (r * cols_n + c) * layers + l

    outs = out_cols.shape[2]
    share = outs // layers
    both = jnp.concatenate([out_cols[:, 0, :], out_cols[:, 0, :]], axis=1)
    want = lax.dynamic_slice_in_dim(both, me_l * share, outs, axis=1).reshape(-1)
    mine = jnp.zeros((row_count, width, share * width), jnp.float32)
    theirs = jnp.zeros((row_count, width, share * width), jnp.float32)
    for s in range(steps):
        left_pairs = []
        right_pairs = []
        for r in range(rows_n):
            for c in range(cols_n):
                for l in range(layers):
                    t = (r + c + s + l * steps) % rows_n
                    left_pairs.append((flat(t, c, l), flat(r, c, l)))
                    right_pairs.append((flat(r, t, l), flat(r, c, l)))
        left = lax.ppermute(payload, ("row", "col", "layer"), left_pairs)
        right = lax.ppermute(payload, ("row", "col", "layer"), right_pairs)
        a_cols = left[row_count, 0, :columns.shape[0]].astype(jnp.int32)
        b_cols = right[row_count, 0, :columns.shape[0]].astype(jnp.int32)
        mine, theirs = one_step(mine, theirs, left, right, a_cols, b_cols, want)

    got = lax.ppermute(theirs, "layer", [(0, 1), (1, 0)])
    return mine[:, :, None, :] + got[:, :, None, :]


def solution(mesh):
    placed = (
        P("col", None, "row", None),
        P("col", "row", None),
        P("col", "row"),
        P("col", "row", None),
    )
    return jax.shard_map(
        per_device,
        mesh=mesh,
        in_specs=placed,
        out_specs=P("col", None, "row", "layer"),
        check_vma=False,
    )
```

```python
import functools

import jax
import jax.numpy as jnp
from jax import lax
from jax.experimental import pallas as pl
from jax.experimental.pallas import tpu as pltpu
from jax.sharding import PartitionSpec as P


def step_kernel(a_cols, b_cols, want, a_ref, b_ref, mine_in, theirs_in, mine_ref, theirs_ref, place_ref, sel_ref):
    width = a_ref.shape[1]
    seg = a_ref.shape[2]
    slots = seg // width
    outs = want.shape[0] // pl.num_programs(0)
    rows = place_ref.shape[0]
    r = pl.program_id(0)

    @pl.when(r == 0)
    def _():
        lane = lax.broadcasted_iota(jnp.int32, (width, 2 * width), 1)
        zero = jnp.zeros((width, 2 * width), b_ref.dtype)

        def fill(k, carry):
            for q in range(slots):
                grp = b_ref[k, :, (q // 2) * 2 * width:(q // 2 + 1) * 2 * width]
                swap = pltpu.roll(grp, width, 1)
                for i in range(2):
                    src = grp if i == q % 2 else swap
                    keep = lane < width if i == 0 else lane >= width
                    place_ref[k, q, i] = jnp.where(keep, src, zero)
            for i in range(2):
                place_ref[k, slots, i] = zero
            return carry

        lax.fori_loop(0, rows, fill, 0)

    for p in range(slots):
        k = a_cols[r * slots + p]
        have = [b_cols[k * slots + q] for q in range(slots)]
        for g in range(outs // 2):
            picks = []
            for i in range(2):
                j = want[r * outs + 2 * g + i]
                hit = jnp.int32(slots)
                for q in range(slots):
                    hit = jnp.where(have[q] == j, jnp.int32(q), hit)
                picks.append(place_ref[k, hit, i])
            sel_ref[p * width:(p + 1) * width, g * 2 * width:(g + 1) * 2 * width] = picks[0] + picks[1]
    prod = jnp.dot(a_ref[0], sel_ref[...], preferred_element_type=jnp.float32)
    half = prod.shape[1] // 2
    mine_ref[0] = mine_in[0] + prod[:, :half]
    theirs_ref[0] = theirs_in[0] + prod[:, half:]


def one_step(mine, theirs, left, right, a_cols, b_cols, want):
    rows, width, seg = mine.shape[0], left.shape[1], left.shape[2]
    outs = want.shape[0] // rows
    block = pl.BlockSpec((1, width, mine.shape[2]), lambda r, *_: (r, 0, 0))
    grid_spec = pltpu.PrefetchScalarGridSpec(
        num_scalar_prefetch=3,
        grid=(rows,),
        in_specs=[
            pl.BlockSpec((1, width, seg), lambda r, *_: (r, 0, 0)),
            pl.BlockSpec(right.shape, lambda r, *_: (0, 0, 0)),
            block,
            block,
        ],
        out_specs=[block, block],
        scratch_shapes=[
            pltpu.VMEM((right.shape[0] - 1, seg // width + 1, 2, width, 2 * width), right.dtype),
            pltpu.VMEM((seg, outs * width), right.dtype),
        ],
    )
    cost = pl.CostEstimate(
        flops=2 * rows * width * seg * outs * width,
        transcendentals=0,
        bytes_accessed=2 * (left.size + right.size) + 8 * (mine.size + theirs.size),
    )
    return pl.pallas_call(
        step_kernel,
        grid_spec=grid_spec,
        out_shape=[jax.ShapeDtypeStruct(mine.shape, mine.dtype)] * 2,
        input_output_aliases={5: 0, 6: 1},
        cost_estimate=cost,
    )(a_cols, b_cols, want, left, right, mine, theirs)


def per_device(x_blocks, x_cols, x_count, out_cols):
    row_count, width, _, lanes = x_blocks.shape
    slots = lanes // width
    values = x_blocks[:, :, 0, :]
    slot_of_lane = lax.broadcasted_iota(jnp.int32, (1, 1, lanes), 2) // width
    values = jnp.where(slot_of_lane < x_count[:, :, None], values, jnp.zeros((), values.dtype))
    columns = x_cols[:, 0, :].reshape(-1)
    extra = jnp.zeros((1, width, lanes), values.dtype)
    extra = extra.at[0, 0, :columns.shape[0]].set(columns.astype(values.dtype))
    payload = jnp.concatenate([values, extra], axis=0)

    rows_n = lax.axis_size("row")
    cols_n = lax.axis_size("col")
    layers = lax.axis_size("layer")
    steps = rows_n // layers
    me_r = lax.axis_index("row")
    me_c = lax.axis_index("col")
    me_l = lax.axis_index("layer")

    def flat(r, c, l):
        return (r * cols_n + c) * layers + l

    outs = out_cols.shape[2]
    share = outs // layers
    both = jnp.concatenate([out_cols[:, 0, :], out_cols[:, 0, :]], axis=1)
    want = lax.dynamic_slice_in_dim(both, me_l * share, outs, axis=1).reshape(-1)
    mine = jnp.zeros((row_count, width, share * width), jnp.float32)
    theirs = jnp.zeros((row_count, width, share * width), jnp.float32)
    for s in range(steps):
        left_pairs = []
        right_pairs = []
        for r in range(rows_n):
            for c in range(cols_n):
                for l in range(layers):
                    t = (r + c + s + l * steps) % rows_n
                    left_pairs.append((flat(t, c, l), flat(r, c, l)))
                    right_pairs.append((flat(r, t, l), flat(r, c, l)))
        left = lax.ppermute(payload, ("row", "col", "layer"), left_pairs)
        right = lax.ppermute(payload, ("row", "col", "layer"), right_pairs)
        a_cols = left[row_count, 0, :columns.shape[0]].astype(jnp.int32)
        b_cols = right[row_count, 0, :columns.shape[0]].astype(jnp.int32)
        mine, theirs = one_step(mine, theirs, left, right, a_cols, b_cols, want)

    got = lax.ppermute(theirs, "layer", [(0, 1), (1, 0)])
    return mine[:, :, None, :] + got[:, :, None, :]


def solution(mesh):
    placed = (
        P("col", None, "row", None),
        P("col", "row", None),
        P("col", "row"),
        P("col", "row", None),
    )
    return jax.shard_map(
        per_device,
        mesh=mesh,
        in_specs=placed,
        out_specs=P("col", None, "row", "layer"),
        check_vma=False,
    )
```

```python
import functools

import jax
import jax.numpy as jnp
from jax import lax
from jax.experimental import pallas as pl
from jax.experimental.pallas import tpu as pltpu
from jax.sharding import PartitionSpec as P


def step_kernel(a_cols, b_cols, want, a_ref, b_ref, mine_in, theirs_in, mine_ref, theirs_ref, place_ref, sel_ref):
    width = a_ref.shape[1]
    seg = a_ref.shape[2]
    slots = seg // width
    outs = want.shape[0] // pl.num_programs(0)
    rows = place_ref.shape[0]
    r = pl.program_id(0)

    @pl.when(r == 0)
    def _():
        lane = lax.broadcasted_iota(jnp.int32, (width, 2 * width), 1)
        zero = jnp.zeros((width, 2 * width), b_ref.dtype)

        def fill(k, carry):
            for q in range(slots):
                grp = b_ref[k, :, (q // 2) * 2 * width:(q // 2 + 1) * 2 * width]
                swap = pltpu.roll(grp, width, 1)
                for i in range(2):
                    src = grp if i == q % 2 else swap
                    keep = lane < width if i == 0 else lane >= width
                    place_ref[k, q, i] = jnp.where(keep, src, zero)
            for i in range(2):
                place_ref[k, slots, i] = zero
            return carry

        lax.fori_loop(0, rows, fill, 0)

    for p in range(slots):
        k = a_cols[r * slots + p]
        have = [b_cols[k * slots + q] for q in range(slots)]
        for g in range(outs // 2):
            picks = []
            for i in range(2):
                j = want[r * outs + 2 * g + i]
                hit = jnp.int32(slots)
                for q in range(slots):
                    hit = jnp.where(have[q] == j, jnp.int32(q), hit)
                picks.append(place_ref[k, hit, i])
            sel_ref[p * width:(p + 1) * width, g * 2 * width:(g + 1) * 2 * width] = picks[0] + picks[1]
    prod = jnp.dot(a_ref[0], sel_ref[...], preferred_element_type=jnp.float32)
    half = prod.shape[1] // 2
    mine_ref[0] = mine_in[0] + prod[:, :half]
    theirs_ref[0] = theirs_in[0] + prod[:, half:]


def one_step(mine, theirs, left, right, a_cols, b_cols, want):
    rows, width, seg = mine.shape[0], left.shape[1], left.shape[2]
    outs = want.shape[0] // rows
    block = pl.BlockSpec((1, width, mine.shape[2]), lambda r, *_: (r, 0, 0))
    grid_spec = pltpu.PrefetchScalarGridSpec(
        num_scalar_prefetch=3,
        grid=(rows,),
        in_specs=[
            pl.BlockSpec((1, width, seg), lambda r, *_: (r, 0, 0)),
            pl.BlockSpec(right.shape, lambda r, *_: (0, 0, 0)),
            block,
            block,
        ],
        out_specs=[block, block],
        scratch_shapes=[
            pltpu.VMEM((right.shape[0] - 1, seg // width + 1, 2, width, 2 * width), right.dtype),
            pltpu.VMEM((seg, outs * width), right.dtype),
        ],
    )
    cost = pl.CostEstimate(
        flops=2 * rows * width * seg * outs * width,
        transcendentals=0,
        bytes_accessed=2 * (left.size + right.size) + 8 * (mine.size + theirs.size),
    )
    return pl.pallas_call(
        step_kernel,
        grid_spec=grid_spec,
        out_shape=[jax.ShapeDtypeStruct(mine.shape, mine.dtype)] * 2,
        input_output_aliases={5: 0, 6: 1},
        cost_estimate=cost,
    )(a_cols, b_cols, want, left, right, mine, theirs)


def per_device(x_blocks, x_cols, x_count, out_cols):
    row_count, width, _, lanes = x_blocks.shape
    slots = lanes // width
    values = x_blocks[:, :, 0, :]
    slot_of_lane = lax.broadcasted_iota(jnp.int32, (1, 1, lanes), 2) // width
    values = jnp.where(slot_of_lane < x_count[:, :, None], values, jnp.zeros((), values.dtype))
    columns = x_cols[:, 0, :].reshape(-1)
    extra = jnp.zeros((1, width, lanes), values.dtype)
    extra = extra.at[0, 0, :columns.shape[0]].set(columns.astype(values.dtype))
    payload = jnp.concatenate([values, extra], axis=0)

    rows_n = lax.axis_size("row")
    cols_n = lax.axis_size("col")
    layers = lax.axis_size("layer")
    steps = rows_n // layers
    me_r = lax.axis_index("row")
    me_c = lax.axis_index("col")
    me_l = lax.axis_index("layer")

    def flat(r, c, l):
        return (r * cols_n + c) * layers + l

    outs = out_cols.shape[2]
    share = outs // layers
    both = jnp.concatenate([out_cols[:, 0, :], out_cols[:, 0, :]], axis=1)
    want = lax.dynamic_slice_in_dim(both, me_l * share, outs, axis=1).reshape(-1)
    mine = jnp.zeros((row_count, width, share * width), jnp.float32)
    theirs = jnp.zeros((row_count, width, share * width), jnp.float32)
    for s in range(steps):
        left_pairs = []
        right_pairs = []
        for r in range(rows_n):
            for c in range(cols_n):
                for l in range(layers):
                    t = (r + c + s + l * steps) % rows_n
                    left_pairs.append((flat(t, c, l), flat(r, c, l)))
                    right_pairs.append((flat(r, t, l), flat(r, c, l)))
        left = lax.ppermute(payload, ("row", "col", "layer"), left_pairs)
        right = lax.ppermute(payload, ("row", "col", "layer"), right_pairs)
        after = (mine[0, 0, 0] * 0).astype(jnp.int32)
        a_cols = left[row_count, 0, :columns.shape[0]].astype(jnp.int32) + after
        b_cols = right[row_count, 0, :columns.shape[0]].astype(jnp.int32) + after
        mine, theirs = one_step(mine, theirs, left, right, a_cols, b_cols, want)

    got = lax.ppermute(theirs, "layer", [(0, 1), (1, 0)])
    return mine[:, :, None, :] + got[:, :, None, :]


def solution(mesh):
    placed = (
        P("col", None, "row", None),
        P("col", "row", None),
        P("col", "row"),
        P("col", "row", None),
    )
    return jax.shard_map(
        per_device,
        mesh=mesh,
        in_specs=placed,
        out_specs=P("col", None, "row", "layer"),
        check_vma=False,
    )
```

```python
import functools

import jax
import jax.numpy as jnp
from jax import lax
from jax.experimental import pallas as pl
from jax.experimental.pallas import tpu as pltpu
from jax.sharding import PartitionSpec as P


def step_kernel(a_cols, b_cols, want, a_ref, b_ref, mine_in, theirs_in, mine_ref, theirs_ref, place_ref, sel_ref):
    width = a_ref.shape[1]
    seg = a_ref.shape[2]
    slots = seg // width
    outs = want.shape[0] // pl.num_programs(0)
    rows = place_ref.shape[0]
    r = pl.program_id(0)

    @pl.when(r == 0)
    def _():
        lane = lax.broadcasted_iota(jnp.int32, (width, 2 * width), 1)
        zero = jnp.zeros((width, 2 * width), b_ref.dtype)

        def fill(k, carry):
            for q in range(slots):
                grp = b_ref[k, :, (q // 2) * 2 * width:(q // 2 + 1) * 2 * width]
                swap = pltpu.roll(grp, width, 1)
                for i in range(2):
                    src = grp if i == q % 2 else swap
                    keep = lane < width if i == 0 else lane >= width
                    place_ref[k, q, i] = jnp.where(keep, src, zero)
            for i in range(2):
                place_ref[k, slots, i] = zero
            return carry

        lax.fori_loop(0, rows, fill, 0)

    for p in range(slots):
        k = a_cols[r * slots + p]
        have = [b_cols[k * slots + q] for q in range(slots)]
        for g in range(outs // 2):
            picks = []
            for i in range(2):
                j = want[r * outs + 2 * g + i]
                hit = jnp.int32(slots)
                for q in range(slots):
                    hit = jnp.where(have[q] == j, jnp.int32(q), hit)
                picks.append(place_ref[k, hit, i])
            sel_ref[p * width:(p + 1) * width, g * 2 * width:(g + 1) * 2 * width] = picks[0] + picks[1]
    prod = jnp.dot(a_ref[0], sel_ref[...], preferred_element_type=jnp.float32)
    half = prod.shape[1] // 2
    mine_ref[0] = mine_in[0] + prod[:, :half]
    theirs_ref[0] = theirs_in[0] + prod[:, half:]


def one_step(mine, theirs, left, right, a_cols, b_cols, want):
    rows, width, seg = mine.shape[0], left.shape[1], left.shape[2]
    outs = want.shape[0] // rows
    block = pl.BlockSpec((1, width, mine.shape[2]), lambda r, *_: (r, 0, 0))
    grid_spec = pltpu.PrefetchScalarGridSpec(
        num_scalar_prefetch=3,
        grid=(rows,),
        in_specs=[
            pl.BlockSpec((1, width, seg), lambda r, *_: (r, 0, 0)),
            pl.BlockSpec(right.shape, lambda r, *_: (0, 0, 0)),
            block,
            block,
        ],
        out_specs=[block, block],
        scratch_shapes=[
            pltpu.VMEM((right.shape[0] - 1, seg // width + 1, 2, width, 2 * width), right.dtype),
            pltpu.VMEM((seg, outs * width), right.dtype),
        ],
    )
    cost = pl.CostEstimate(
        flops=2 * rows * width * seg * outs * width,
        transcendentals=0,
        bytes_accessed=2 * (left.size + right.size) + 8 * (mine.size + theirs.size),
    )
    return pl.pallas_call(
        step_kernel,
        grid_spec=grid_spec,
        out_shape=[jax.ShapeDtypeStruct(mine.shape, mine.dtype)] * 2,
        input_output_aliases={5: 0, 6: 1},
        cost_estimate=cost,
    )(a_cols, b_cols, want, left, right, mine, theirs)


def per_device(x_blocks, x_cols, x_count, out_cols):
    row_count, width, _, lanes = x_blocks.shape
    slots = lanes // width
    values = x_blocks[:, :, 0, :]
    slot_of_lane = lax.broadcasted_iota(jnp.int32, (1, 1, lanes), 2) // width
    values = jnp.where(slot_of_lane < x_count[:, :, None], values, jnp.zeros((), values.dtype))
    columns = x_cols[:, 0, :].reshape(-1)
    extra = jnp.zeros((1, width, lanes), values.dtype)
    extra = extra.at[0, 0, :columns.shape[0]].set(columns.astype(values.dtype))
    payload = jnp.concatenate([values, extra], axis=0)

    rows_n = lax.axis_size("row")
    cols_n = lax.axis_size("col")
    layers = lax.axis_size("layer")
    steps = rows_n // layers
    me_r = lax.axis_index("row")
    me_c = lax.axis_index("col")
    me_l = lax.axis_index("layer")

    def flat(r, c, l):
        return (r * cols_n + c) * layers + l

    outs = out_cols.shape[2]
    share = outs // layers
    both = jnp.concatenate([out_cols[:, 0, :], out_cols[:, 0, :]], axis=1)
    want = lax.dynamic_slice_in_dim(both, me_l * share, outs, axis=1).reshape(-1)
    mine = jnp.zeros((row_count, width, share * width), jnp.float32)
    theirs = jnp.zeros((row_count, width, share * width), jnp.float32)
    for s in range(steps):
        left_pairs = []
        right_pairs = []
        for r in range(rows_n):
            for c in range(cols_n):
                for l in range(layers):
                    t = (r + c + s + l * steps) % rows_n
                    left_pairs.append((flat(t, c, l), flat(r, c, l)))
                    right_pairs.append((flat(r, t, l), flat(r, c, l)))
        left = lax.ppermute(payload, ("row", "col", "layer"), left_pairs)
        right = lax.ppermute(payload, ("row", "col", "layer"), right_pairs)
        payload = payload + (left[0, 0, 0] * 0 + right[0, 0, 0] * 0)
        after = (mine[0, 0, 0] * 0).astype(jnp.int32)
        a_cols = left[row_count, 0, :columns.shape[0]].astype(jnp.int32) + after
        b_cols = right[row_count, 0, :columns.shape[0]].astype(jnp.int32) + after
        mine, theirs = one_step(mine, theirs, left, right, a_cols, b_cols, want)

    got = lax.ppermute(theirs, "layer", [(0, 1), (1, 0)])
    return mine[:, :, None, :] + got[:, :, None, :]


def solution(mesh):
    placed = (
        P("col", None, "row", None),
        P("col", "row", None),
        P("col", "row"),
        P("col", "row", None),
    )
    return jax.shard_map(
        per_device,
        mesh=mesh,
        in_specs=placed,
        out_specs=P("col", None, "row", "layer"),
        check_vma=False,
    )
```

```python
import functools

import jax
import jax.numpy as jnp
from jax import lax
from jax.experimental import pallas as pl
from jax.experimental.pallas import tpu as pltpu
from jax.sharding import PartitionSpec as P


def step_kernel(a_cols, b_cols, want, a_ref, b_ref, *refs):
    if len(refs) == 7:
        mine_in, theirs_in, mine_ref, theirs_ref, place_ref, sel_ref, slot_of = refs
    else:
        mine_in = theirs_in = None
        mine_ref, theirs_ref, place_ref, sel_ref, slot_of = refs
    width = a_ref.shape[1]
    seg = a_ref.shape[2]
    slots = seg // width
    outs = want.shape[0] // pl.num_programs(0)
    rows = place_ref.shape[0]
    r = pl.program_id(0)

    @pl.when(r == 0)
    def _():
        lane = lax.broadcasted_iota(jnp.int32, (width, 2 * width), 1)
        zero = jnp.zeros((width, 2 * width), b_ref.dtype)

        def fill(k, carry):
            for q in range(slots):
                grp = b_ref[k, :, (q // 2) * 2 * width:(q // 2 + 1) * 2 * width]
                swap = pltpu.roll(grp, width, 1)
                for i in range(2):
                    src = grp if i == q % 2 else swap
                    keep = lane < width if i == 0 else lane >= width
                    place_ref[k, q, i] = jnp.where(keep, src, zero)
            for i in range(2):
                place_ref[k, slots, i] = zero
            return carry

        lax.fori_loop(0, rows, fill, 0)
        for n in range(rows * rows):
            slot_of[n] = jnp.int32(slots)
        for n in range(rows * slots):
            slot_of[(n // slots) * rows + b_cols[n]] = jnp.int32(n % slots)

    for p in range(slots):
        k = a_cols[r * slots + p]
        for g in range(outs // 2):
            picks = []
            for i in range(2):
                hit = slot_of[k * rows + want[r * outs + 2 * g + i]]
                picks.append(place_ref[k, hit, i])
            sel_ref[p * width:(p + 1) * width, g * 2 * width:(g + 1) * 2 * width] = picks[0] + picks[1]
    prod = jnp.dot(a_ref[0], sel_ref[...], preferred_element_type=jnp.float32)
    half = prod.shape[1] // 2
    if mine_in is None:
        mine_ref[0] = prod[:, :half]
        theirs_ref[0] = prod[:, half:]
    else:
        mine_ref[0] = mine_in[0] + prod[:, :half]
        theirs_ref[0] = theirs_in[0] + prod[:, half:]


def one_step(mine, theirs, left, right, a_cols, b_cols, want):
    rows, width, seg = left.shape[0] - 1, left.shape[1], left.shape[2]
    outs = want.shape[0] // rows
    share = outs // 2 * width
    block = pl.BlockSpec((1, width, share), lambda r, *_: (r, 0, 0))
    sums = [] if mine is None else [mine, theirs]
    grid_spec = pltpu.PrefetchScalarGridSpec(
        num_scalar_prefetch=3,
        grid=(rows,),
        in_specs=[
            pl.BlockSpec((1, width, seg), lambda r, *_: (r, 0, 0)),
            pl.BlockSpec(right.shape, lambda r, *_: (0, 0, 0)),
        ] + [block] * len(sums),
        out_specs=[block, block],
        scratch_shapes=[
            pltpu.VMEM((right.shape[0] - 1, seg // width + 1, 2, width, 2 * width), right.dtype),
            pltpu.VMEM((seg, outs * width), right.dtype),
            pltpu.SMEM(((right.shape[0] - 1) ** 2,), jnp.int32),
        ],
    )
    cost = pl.CostEstimate(
        flops=2 * rows * width * seg * outs * width,
        transcendentals=0,
        bytes_accessed=2 * (left.size + right.size) + 4 * (2 + len(sums)) * rows * width * share,
    )
    return pl.pallas_call(
        step_kernel,
        grid_spec=grid_spec,
        out_shape=[jax.ShapeDtypeStruct((rows, width, share), jnp.float32)] * 2,
        input_output_aliases={5: 0, 6: 1} if sums else {},
        cost_estimate=cost,
    )(a_cols, b_cols, want, left, right, *sums)


def per_device(x_blocks, x_cols, x_count, out_cols):
    row_count, width, _, lanes = x_blocks.shape
    slots = lanes // width
    values = x_blocks[:, :, 0, :]
    slot_of_lane = lax.broadcasted_iota(jnp.int32, (1, 1, lanes), 2) // width
    values = jnp.where(slot_of_lane < x_count[:, :, None], values, jnp.zeros((), values.dtype))
    columns = x_cols[:, 0, :].reshape(-1)
    extra = jnp.zeros((1, width, lanes), values.dtype)
    extra = extra.at[0, 0, :columns.shape[0]].set(columns.astype(values.dtype))
    payload = jnp.concatenate([values, extra], axis=0)

    rows_n = lax.axis_size("row")
    cols_n = lax.axis_size("col")
    layers = lax.axis_size("layer")
    steps = rows_n // layers
    me_r = lax.axis_index("row")
    me_c = lax.axis_index("col")
    me_l = lax.axis_index("layer")

    def flat(r, c, l):
        return (r * cols_n + c) * layers + l

    outs = out_cols.shape[2]
    share = outs // layers
    both = jnp.concatenate([out_cols[:, 0, :], out_cols[:, 0, :]], axis=1)
    want = lax.dynamic_slice_in_dim(both, me_l * share, outs, axis=1).reshape(-1)
    mine = theirs = None
    for s in range(steps):
        left_pairs = []
        right_pairs = []
        for r in range(rows_n):
            for c in range(cols_n):
                for l in range(layers):
                    t = (r + c + s + l * steps) % rows_n
                    left_pairs.append((flat(t, c, l), flat(r, c, l)))
                    right_pairs.append((flat(r, t, l), flat(r, c, l)))
        left = lax.ppermute(payload, ("row", "col", "layer"), left_pairs)
        right = lax.ppermute(payload, ("row", "col", "layer"), right_pairs)
        after = 0 if mine is None else (mine[0, 0, 0] * 0).astype(jnp.int32)
        a_cols = left[row_count, 0, :columns.shape[0]].astype(jnp.int32) + after
        b_cols = right[row_count, 0, :columns.shape[0]].astype(jnp.int32) + after
        mine, theirs = one_step(mine, theirs, left, right, a_cols, b_cols, want)

    got = lax.ppermute(theirs, "layer", [(0, 1), (1, 0)])
    return mine[:, :, None, :] + got[:, :, None, :]


def solution(mesh):
    placed = (
        P("col", None, "row", None),
        P("col", "row", None),
        P("col", "row"),
        P("col", "row", None),
    )
    return jax.shard_map(
        per_device,
        mesh=mesh,
        in_specs=placed,
        out_specs=P("col", None, "row", "layer"),
        check_vma=False,
    )
```

```python
import functools

import jax
import jax.numpy as jnp
from jax import lax
from jax.experimental import pallas as pl
from jax.experimental.pallas import tpu as pltpu
from jax.sharding import PartitionSpec as P


def step_kernel(a_cols, b_cols, want, a_ref, b_ref, *refs):
    if len(refs) == 7:
        mine_in, theirs_in, mine_ref, theirs_ref, place_ref, sel_ref, slot_of = refs
    else:
        mine_in = theirs_in = None
        mine_ref, theirs_ref, place_ref, sel_ref, slot_of = refs
    width = a_ref.shape[1]
    seg = a_ref.shape[2]
    slots = seg // width
    rows = place_ref.shape[0]
    outs = want.shape[0] // rows
    lane = lax.broadcasted_iota(jnp.int32, (width, 2 * width), 1)
    zero = jnp.zeros((width, 2 * width), b_ref.dtype)

    def fill(k, carry):
        for q in range(slots):
            grp = b_ref[k, :, (q // 2) * 2 * width:(q // 2 + 1) * 2 * width]
            swap = pltpu.roll(grp, width, 1)
            for i in range(2):
                src = grp if i == q % 2 else swap
                keep = lane < width if i == 0 else lane >= width
                place_ref[k, q, i] = jnp.where(keep, src, zero)
        for i in range(2):
            place_ref[k, slots, i] = zero
        return carry

    lax.fori_loop(0, rows, fill, 0)
    for n in range(rows * rows):
        slot_of[n] = jnp.int32(slots)
    for n in range(rows * slots):
        slot_of[(n // slots) * rows + b_cols[n]] = jnp.int32(n % slots)

    def one_row(r, carry):
        for p in range(slots):
            k = a_cols[r * slots + p]
            for g in range(outs // 2):
                picks = []
                for i in range(2):
                    hit = slot_of[k * rows + want[r * outs + 2 * g + i]]
                    picks.append(place_ref[k, hit, i])
                sel_ref[p * width:(p + 1) * width, g * 2 * width:(g + 1) * 2 * width] = picks[0] + picks[1]
        prod = jnp.dot(a_ref[r], sel_ref[...], preferred_element_type=jnp.float32)
        half = prod.shape[1] // 2
        if mine_in is None:
            mine_ref[r] = prod[:, :half]
            theirs_ref[r] = prod[:, half:]
        else:
            mine_ref[r] = mine_in[r] + prod[:, :half]
            theirs_ref[r] = theirs_in[r] + prod[:, half:]
        return carry

    lax.fori_loop(0, rows, one_row, 0)


def one_step(mine, theirs, left, right, a_cols, b_cols, want):
    rows, width, seg = left.shape[0] - 1, left.shape[1], left.shape[2]
    outs = want.shape[0] // rows
    share = outs // 2 * width
    sums = [] if mine is None else [mine, theirs]
    smem = pl.BlockSpec(memory_space=pltpu.SMEM)
    vmem = pl.BlockSpec(memory_space=pltpu.VMEM)
    cost = pl.CostEstimate(
        flops=2 * rows * width * seg * outs * width,
        transcendentals=0,
        bytes_accessed=2 * (left.size + right.size) + 4 * (2 + len(sums)) * rows * width * share,
    )
    return pl.pallas_call(
        step_kernel,
        in_specs=[smem] * 3 + [vmem] * (2 + len(sums)),
        out_specs=[vmem, vmem],
        scratch_shapes=[
            pltpu.VMEM((rows, seg // width + 1, 2, width, 2 * width), right.dtype),
            pltpu.VMEM((seg, outs * width), right.dtype),
            pltpu.SMEM((rows * rows,), jnp.int32),
        ],
        out_shape=[jax.ShapeDtypeStruct((rows, width, share), jnp.float32)] * 2,
        input_output_aliases={5: 0, 6: 1} if sums else {},
        cost_estimate=cost,
    )(a_cols, b_cols, want, left, right, *sums)


def per_device(x_blocks, x_cols, x_count, out_cols):
    row_count, width, _, lanes = x_blocks.shape
    slots = lanes // width
    values = x_blocks[:, :, 0, :]
    slot_of_lane = lax.broadcasted_iota(jnp.int32, (1, 1, lanes), 2) // width
    values = jnp.where(slot_of_lane < x_count[:, :, None], values, jnp.zeros((), values.dtype))
    columns = x_cols[:, 0, :].reshape(-1)
    extra = jnp.zeros((1, width, lanes), values.dtype)
    extra = extra.at[0, 0, :columns.shape[0]].set(columns.astype(values.dtype))
    payload = jnp.concatenate([values, extra], axis=0)

    rows_n = lax.axis_size("row")
    cols_n = lax.axis_size("col")
    layers = lax.axis_size("layer")
    steps = rows_n // layers
    me_r = lax.axis_index("row")
    me_c = lax.axis_index("col")
    me_l = lax.axis_index("layer")

    def flat(r, c, l):
        return (r * cols_n + c) * layers + l

    outs = out_cols.shape[2]
    share = outs // layers
    both = jnp.concatenate([out_cols[:, 0, :], out_cols[:, 0, :]], axis=1)
    want = lax.dynamic_slice_in_dim(both, me_l * share, outs, axis=1).reshape(-1)
    mine = theirs = None
    for s in range(steps):
        left_pairs = []
        right_pairs = []
        for r in range(rows_n):
            for c in range(cols_n):
                for l in range(layers):
                    t = (r + c + s + l * steps) % rows_n
                    left_pairs.append((flat(t, c, l), flat(r, c, l)))
                    right_pairs.append((flat(r, t, l), flat(r, c, l)))
        left = lax.ppermute(payload, ("row", "col", "layer"), left_pairs)
        right = lax.ppermute(payload, ("row", "col", "layer"), right_pairs)
        after = 0 if mine is None else (mine[0, 0, 0] * 0).astype(jnp.int32)
        a_cols = left[row_count, 0, :columns.shape[0]].astype(jnp.int32) + after
        b_cols = right[row_count, 0, :columns.shape[0]].astype(jnp.int32) + after
        mine, theirs = one_step(mine, theirs, left, right, a_cols, b_cols, want)

    got = lax.ppermute(theirs, "layer", [(0, 1), (1, 0)])
    return mine[:, :, None, :] + got[:, :, None, :]


def solution(mesh):
    placed = (
        P("col", None, "row", None),
        P("col", "row", None),
        P("col", "row"),
        P("col", "row", None),
    )
    return jax.shard_map(
        per_device,
        mesh=mesh,
        in_specs=placed,
        out_specs=P("col", None, "row", "layer"),
        check_vma=False,
    )
```

```python
import functools

import jax
import jax.numpy as jnp
from jax import lax
from jax.experimental import pallas as pl
from jax.experimental.pallas import tpu as pltpu
from jax.sharding import PartitionSpec as P


def step_kernel(a_cols, b_cols, want, a_ref, b_ref, *refs):
    if len(refs) == 7:
        mine_in, theirs_in, mine_ref, theirs_ref, place_ref, sel_ref, slot_of = refs
    else:
        mine_in = theirs_in = None
        mine_ref, theirs_ref, place_ref, sel_ref, slot_of = refs
    width = a_ref.shape[1]
    seg = a_ref.shape[2]
    slots = seg // width
    rows = place_ref.shape[0]
    outs = want.shape[0] // rows
    lane = lax.broadcasted_iota(jnp.int32, (width, 2 * width), 1)
    zero = jnp.zeros((width, 2 * width), b_ref.dtype)

    def fill(k, carry):
        for q in range(slots):
            grp = b_ref[k, :, (q // 2) * 2 * width:(q // 2 + 1) * 2 * width]
            swap = pltpu.roll(grp, width, 1)
            for i in range(2):
                src = grp if i == q % 2 else swap
                keep = lane < width if i == 0 else lane >= width
                place_ref[k, q, i] = jnp.where(keep, src, zero)
        for i in range(2):
            place_ref[k, slots, i] = zero
        return carry

    lax.fori_loop(0, rows, fill, 0)
    for n in range(rows * rows):
        slot_of[n] = jnp.int32(slots)
    for n in range(rows * slots):
        slot_of[(n // slots) * rows + b_cols[n]] = jnp.int32(n % slots)

    def one_row(r, sel_ref):
        for p in range(slots):
            k = a_cols[r * slots + p]
            for g in range(outs // 2):
                picks = []
                for i in range(2):
                    hit = slot_of[k * rows + want[r * outs + 2 * g + i]]
                    picks.append(place_ref[k, hit, i])
                sel_ref[p * width:(p + 1) * width, g * 2 * width:(g + 1) * 2 * width] = picks[0] + picks[1]
        prod = jnp.dot(a_ref[r], sel_ref[...], preferred_element_type=jnp.float32)
        half = prod.shape[1] // 2
        if mine_in is None:
            mine_ref[r] = prod[:, :half]
            theirs_ref[r] = prod[:, half:]
        else:
            mine_ref[r] = mine_in[r] + prod[:, :half]
            theirs_ref[r] = theirs_in[r] + prod[:, half:]

    group = sel_ref.shape[0]

    def some_rows(n, carry):
        for m in range(group):
            one_row(group * n + m, sel_ref.at[m])
        return carry

    lax.fori_loop(0, rows // group, some_rows, 0)


def one_step(mine, theirs, left, right, a_cols, b_cols, want):
    rows, width, seg = left.shape[0] - 1, left.shape[1], left.shape[2]
    outs = want.shape[0] // rows
    share = outs // 2 * width
    sums = [] if mine is None else [mine, theirs]
    smem = pl.BlockSpec(memory_space=pltpu.SMEM)
    vmem = pl.BlockSpec(memory_space=pltpu.VMEM)
    cost = pl.CostEstimate(
        flops=2 * rows * width * seg * outs * width,
        transcendentals=0,
        bytes_accessed=2 * (left.size + right.size) + 4 * (2 + len(sums)) * rows * width * share,
    )
    return pl.pallas_call(
        step_kernel,
        in_specs=[smem] * 3 + [vmem] * (2 + len(sums)),
        out_specs=[vmem, vmem],
        scratch_shapes=[
            pltpu.VMEM((rows, seg // width + 1, 2, width, 2 * width), right.dtype),
            pltpu.VMEM((4 if rows % 4 == 0 else 1, seg, outs * width), right.dtype),
            pltpu.SMEM((rows * rows,), jnp.int32),
        ],
        out_shape=[jax.ShapeDtypeStruct((rows, width, share), jnp.float32)] * 2,
        input_output_aliases={5: 0, 6: 1} if sums else {},
        cost_estimate=cost,
    )(a_cols, b_cols, want, left, right, *sums)


def per_device(x_blocks, x_cols, x_count, out_cols):
    row_count, width, _, lanes = x_blocks.shape
    slots = lanes // width
    values = x_blocks[:, :, 0, :]
    slot_of_lane = lax.broadcasted_iota(jnp.int32, (1, 1, lanes), 2) // width
    values = jnp.where(slot_of_lane < x_count[:, :, None], values, jnp.zeros((), values.dtype))
    columns = x_cols[:, 0, :].reshape(-1)
    extra = jnp.zeros((1, width, lanes), values.dtype)
    extra = extra.at[0, 0, :columns.shape[0]].set(columns.astype(values.dtype))
    payload = jnp.concatenate([values, extra], axis=0)

    rows_n = lax.axis_size("row")
    cols_n = lax.axis_size("col")
    layers = lax.axis_size("layer")
    steps = rows_n // layers
    me_r = lax.axis_index("row")
    me_c = lax.axis_index("col")
    me_l = lax.axis_index("layer")

    def flat(r, c, l):
        return (r * cols_n + c) * layers + l

    outs = out_cols.shape[2]
    share = outs // layers
    both = jnp.concatenate([out_cols[:, 0, :], out_cols[:, 0, :]], axis=1)
    want = lax.dynamic_slice_in_dim(both, me_l * share, outs, axis=1).reshape(-1)
    mine = theirs = None
    for s in range(steps):
        left_pairs = []
        right_pairs = []
        for r in range(rows_n):
            for c in range(cols_n):
                for l in range(layers):
                    t = (r + c + s + l * steps) % rows_n
                    left_pairs.append((flat(t, c, l), flat(r, c, l)))
                    right_pairs.append((flat(r, t, l), flat(r, c, l)))
        left = lax.ppermute(payload, ("row", "col", "layer"), left_pairs)
        right = lax.ppermute(payload, ("row", "col", "layer"), right_pairs)
        after = 0 if mine is None else (mine[0, 0, 0] * 0).astype(jnp.int32)
        a_cols = left[row_count, 0, :columns.shape[0]].astype(jnp.int32) + after
        b_cols = right[row_count, 0, :columns.shape[0]].astype(jnp.int32) + after
        mine, theirs = one_step(mine, theirs, left, right, a_cols, b_cols, want)

    got = lax.ppermute(theirs, "layer", [(0, 1), (1, 0)])
    return mine[:, :, None, :] + got[:, :, None, :]


def solution(mesh):
    placed = (
        P("col", None, "row", None),
        P("col", "row", None),
        P("col", "row"),
        P("col", "row", None),
    )
    return jax.shard_map(
        per_device,
        mesh=mesh,
        in_specs=placed,
        out_specs=P("col", None, "row", "layer"),
        check_vma=False,
    )
```

```python
import functools

import jax
import jax.numpy as jnp
from jax import lax
from jax.experimental import pallas as pl
from jax.experimental.pallas import tpu as pltpu
from jax.sharding import PartitionSpec as P


def step_kernel(a_cols, b_cols, want, a_ref, b_ref, *refs):
    if len(refs) == 8:
        mine_in, theirs_in, mine_ref, theirs_ref, tick, place_ref, sel_ref, slot_of = refs
    else:
        mine_in = theirs_in = None
        mine_ref, theirs_ref, tick, place_ref, sel_ref, slot_of = refs
    width = a_ref.shape[1]
    seg = a_ref.shape[2]
    slots = seg // width
    rows = place_ref.shape[0]
    outs = want.shape[0] // rows
    lane = lax.broadcasted_iota(jnp.int32, (width, 2 * width), 1)
    zero = jnp.zeros((width, 2 * width), b_ref.dtype)
    tick[0] = jnp.int32(0)

    def fill(k, carry):
        for q in range(slots):
            grp = b_ref[k, :, (q // 2) * 2 * width:(q // 2 + 1) * 2 * width]
            swap = pltpu.roll(grp, width, 1)
            for i in range(2):
                src = grp if i == q % 2 else swap
                keep = lane < width if i == 0 else lane >= width
                place_ref[k, q, i] = jnp.where(keep, src, zero)
        for i in range(2):
            place_ref[k, slots, i] = zero
        return carry

    lax.fori_loop(0, rows, fill, 0)
    for n in range(rows * rows):
        slot_of[n] = jnp.int32(slots)
    for n in range(rows * slots):
        slot_of[(n // slots) * rows + b_cols[n]] = jnp.int32(n % slots)

    def one_row(r, sel_ref):
        for p in range(slots):
            k = a_cols[r * slots + p]
            for g in range(outs // 2):
                picks = []
                for i in range(2):
                    hit = slot_of[k * rows + want[r * outs + 2 * g + i]]
                    picks.append(place_ref[k, hit, i])
                sel_ref[p * width:(p + 1) * width, g * 2 * width:(g + 1) * 2 * width] = picks[0] + picks[1]
        prod = jnp.dot(a_ref[r], sel_ref[...], preferred_element_type=jnp.float32)
        half = prod.shape[1] // 2
        if mine_in is None:
            mine_ref[r] = prod[:, :half]
            theirs_ref[r] = prod[:, half:]
        else:
            mine_ref[r] = mine_in[r] + prod[:, :half]
            theirs_ref[r] = theirs_in[r] + prod[:, half:]

    group = sel_ref.shape[0]

    def some_rows(n, carry):
        for m in range(group):
            one_row(group * n + m, sel_ref.at[m])
        return carry

    lax.fori_loop(0, rows // group, some_rows, 0)


def one_step(mine, theirs, left, right, a_cols, b_cols, want):
    rows, width, seg = left.shape[0] - 1, left.shape[1], left.shape[2]
    outs = want.shape[0] // rows
    share = outs // 2 * width
    sums = [] if mine is None else [mine, theirs]
    smem = pl.BlockSpec(memory_space=pltpu.SMEM)
    vmem = pl.BlockSpec(memory_space=pltpu.VMEM)
    cost = pl.CostEstimate(
        flops=2 * rows * width * seg * outs * width,
        transcendentals=0,
        bytes_accessed=2 * (left.size + right.size) + 4 * (2 + len(sums)) * rows * width * share,
    )
    return pl.pallas_call(
        step_kernel,
        in_specs=[smem] * 3 + [vmem] * (2 + len(sums)),
        out_specs=[vmem, vmem, smem],
        scratch_shapes=[
            pltpu.VMEM((rows, seg // width + 1, 2, width, 2 * width), right.dtype),
            pltpu.VMEM((4 if rows % 4 == 0 else 1, seg, outs * width), right.dtype),
            pltpu.SMEM((rows * rows,), jnp.int32),
        ],
        out_shape=[jax.ShapeDtypeStruct((rows, width, share), jnp.float32)] * 2
        + [jax.ShapeDtypeStruct((1,), jnp.int32)],
        input_output_aliases={5: 0, 6: 1} if sums else {},
        cost_estimate=cost,
    )(a_cols, b_cols, want, left, right, *sums)


def per_device(x_blocks, x_cols, x_count, out_cols):
    row_count, width, _, lanes = x_blocks.shape
    slots = lanes // width
    values = x_blocks[:, :, 0, :]
    slot_of_lane = lax.broadcasted_iota(jnp.int32, (1, 1, lanes), 2) // width
    values = jnp.where(slot_of_lane < x_count[:, :, None], values, jnp.zeros((), values.dtype))
    columns = x_cols[:, 0, :].reshape(-1)
    extra = jnp.zeros((1, width, lanes), values.dtype)
    extra = extra.at[0, 0, :columns.shape[0]].set(columns.astype(values.dtype))
    payload = jnp.concatenate([values, extra], axis=0)

    rows_n = lax.axis_size("row")
    cols_n = lax.axis_size("col")
    layers = lax.axis_size("layer")
    steps = rows_n // layers
    me_r = lax.axis_index("row")
    me_c = lax.axis_index("col")
    me_l = lax.axis_index("layer")

    def flat(r, c, l):
        return (r * cols_n + c) * layers + l

    outs = out_cols.shape[2]
    share = outs // layers
    both = jnp.concatenate([out_cols[:, 0, :], out_cols[:, 0, :]], axis=1)
    want = lax.dynamic_slice_in_dim(both, me_l * share, outs, axis=1).reshape(-1)
    mine = theirs = None
    tick = jnp.zeros((1,), jnp.int32)
    for s in range(steps):
        left_pairs = []
        right_pairs = []
        for r in range(rows_n):
            for c in range(cols_n):
                for l in range(layers):
                    t = (r + c + s + l * steps) % rows_n
                    left_pairs.append((flat(t, c, l), flat(r, c, l)))
                    right_pairs.append((flat(r, t, l), flat(r, c, l)))
        left = lax.ppermute(payload, ("row", "col", "layer"), left_pairs)
        right = lax.ppermute(payload, ("row", "col", "layer"), right_pairs)
        n = columns.shape[0]
        a_cols = left[row_count, 0, :n].astype(jnp.int32) + tick
        b_cols = right[row_count, 0, :n].astype(jnp.int32) + tick
        mine, theirs, tick = one_step(mine, theirs, left, right, a_cols, b_cols, want)

    got = lax.ppermute(theirs, "layer", [(0, 1), (1, 0)])
    return mine[:, :, None, :] + got[:, :, None, :]


def solution(mesh):
    placed = (
        P("col", None, "row", None),
        P("col", "row", None),
        P("col", "row"),
        P("col", "row", None),
    )
    return jax.shard_map(
        per_device,
        mesh=mesh,
        in_specs=placed,
        out_specs=P("col", None, "row", "layer"),
        check_vma=False,
    )
```

```python
import functools

import jax
import jax.numpy as jnp
from jax import lax
from jax.experimental import pallas as pl
from jax.experimental.pallas import tpu as pltpu
from jax.sharding import PartitionSpec as P


def step_kernel(a_cols, b_cols, want, a_ref, b_ref, *refs):
    if len(refs) == 8:
        mine_in, theirs_in, mine_ref, theirs_ref, tick, place_ref, sel_ref, slot_of = refs
    else:
        mine_in = theirs_in = None
        mine_ref, theirs_ref, tick, place_ref, sel_ref, slot_of = refs
    width = a_ref.shape[1]
    seg = a_ref.shape[2]
    slots = seg // width
    rows = place_ref.shape[0]
    outs = want.shape[0] // rows
    lane = lax.broadcasted_iota(jnp.int32, (width, 2 * width), 1)
    zero = jnp.zeros((width, 2 * width), b_ref.dtype)
    tick[0] = jnp.int32(0)

    def fill(k, carry):
        for q in range(slots):
            grp = b_ref[k, :, (q // 2) * 2 * width:(q // 2 + 1) * 2 * width]
            swap = pltpu.roll(grp, width, 1)
            for i in range(2):
                src = grp if i == q % 2 else swap
                keep = lane < width if i == 0 else lane >= width
                place_ref[k, q, i] = jnp.where(keep, src, zero)
        for i in range(2):
            place_ref[k, slots, i] = zero
        return carry

    lax.fori_loop(0, rows, fill, 0)
    for n in range(rows * rows):
        slot_of[n] = jnp.int32(slots)
    for n in range(rows * slots):
        slot_of[(n // slots) * rows + b_cols[n]] = jnp.int32(n % slots)

    def one_row(r, sel_ref):
        for p in range(slots):
            k = a_cols[r * slots + p]
            for g in range(outs // 2):
                picks = []
                for i in range(2):
                    hit = slot_of[k * rows + want[r * outs + 2 * g + i]]
                    picks.append(place_ref[k, hit, i])
                sel_ref[p * width:(p + 1) * width, g * 2 * width:(g + 1) * 2 * width] = picks[0] + picks[1]
        prod = jnp.dot(a_ref[r], sel_ref[...], preferred_element_type=jnp.float32)
        half = prod.shape[1] // 2
        if mine_in is None:
            mine_ref[r] = prod[:, :half]
            theirs_ref[r] = prod[:, half:]
        else:
            mine_ref[r] = mine_in[r] + prod[:, :half]
            theirs_ref[r] = theirs_in[r] + prod[:, half:]

    group = sel_ref.shape[0]

    def some_rows(n, carry):
        for m in range(group):
            one_row(group * n + m, sel_ref.at[m])
        return carry

    lax.fori_loop(0, rows // group, some_rows, 0)


def one_step(mine, theirs, left, right, a_cols, b_cols, want):
    rows, width, seg = left.shape[0] - 1, left.shape[1], left.shape[2]
    outs = want.shape[0] // rows
    share = outs // 2 * width
    sums = [] if mine is None else [mine, theirs]
    smem = pl.BlockSpec(memory_space=pltpu.SMEM)
    vmem = pl.BlockSpec(memory_space=pltpu.VMEM)
    cost = pl.CostEstimate(
        flops=2 * rows * width * seg * outs * width,
        transcendentals=0,
        bytes_accessed=2 * (left.size + right.size) + 4 * (2 + len(sums)) * rows * width * share,
    )
    return pl.pallas_call(
        step_kernel,
        in_specs=[smem] * 3 + [vmem] * (2 + len(sums)),
        out_specs=[vmem, vmem, smem],
        scratch_shapes=[
            pltpu.VMEM((rows, seg // width + 1, 2, width, 2 * width), right.dtype),
            pltpu.VMEM((4 if rows % 4 == 0 else 1, seg, outs * width), right.dtype),
            pltpu.SMEM((rows * rows,), jnp.int32),
        ],
        out_shape=[jax.ShapeDtypeStruct((rows, width, share), jnp.float32)] * 2
        + [jax.ShapeDtypeStruct((1,), jnp.int32)],
        input_output_aliases={5: 0, 6: 1} if sums else {},
        cost_estimate=cost,
    )(a_cols, b_cols, want, left, right, *sums)


def per_device(x_blocks, x_cols, x_count, out_cols):
    row_count, width, _, lanes = x_blocks.shape
    slots = lanes // width
    values = x_blocks[:, :, 0, :]
    slot_of_lane = lax.broadcasted_iota(jnp.int32, (1, 1, lanes), 2) // width
    values = jnp.where(slot_of_lane < x_count[:, :, None], values, jnp.zeros((), values.dtype))
    columns = x_cols[:, 0, :].reshape(-1)
    extra = jnp.zeros((1, width, lanes), values.dtype)
    extra = extra.at[0, 0, :columns.shape[0]].set(columns.astype(values.dtype))
    payload = jnp.concatenate([values, extra], axis=0)

    rows_n = lax.axis_size("row")
    cols_n = lax.axis_size("col")
    layers = lax.axis_size("layer")
    steps = rows_n // layers
    me_r = lax.axis_index("row")
    me_c = lax.axis_index("col")
    me_l = lax.axis_index("layer")

    def flat(r, c, l):
        return (r * cols_n + c) * layers + l

    outs = out_cols.shape[2]
    share = outs // layers
    both = jnp.concatenate([out_cols[:, 0, :], out_cols[:, 0, :]], axis=1)
    want = lax.dynamic_slice_in_dim(both, me_l * share, outs, axis=1).reshape(-1)
    mine = theirs = None
    tick = jnp.zeros((1,), jnp.int32)
    for s in range(steps):
        left_pairs = []
        right_pairs = []
        for r in range(rows_n):
            for c in range(cols_n):
                for l in range(layers):
                    t = r ^ c ^ (s + l * steps)
                    left_pairs.append((flat(t, c, l), flat(r, c, l)))
                    right_pairs.append((flat(r, t, l), flat(r, c, l)))
        left = lax.ppermute(payload, ("row", "col", "layer"), left_pairs)
        right = lax.ppermute(payload, ("row", "col", "layer"), right_pairs)
        n = columns.shape[0]
        a_cols = left[row_count, 0, :n].astype(jnp.int32) + tick
        b_cols = right[row_count, 0, :n].astype(jnp.int32) + tick
        mine, theirs, tick = one_step(mine, theirs, left, right, a_cols, b_cols, want)

    got = lax.ppermute(theirs, "layer", [(0, 1), (1, 0)])
    return mine[:, :, None, :] + got[:, :, None, :]


def solution(mesh):
    placed = (
        P("col", None, "row", None),
        P("col", "row", None),
        P("col", "row"),
        P("col", "row", None),
    )
    return jax.shard_map(
        per_device,
        mesh=mesh,
        in_specs=placed,
        out_specs=P("col", None, "row", "layer"),
        check_vma=False,
    )
```

```python
import functools

import jax
import jax.numpy as jnp
from jax import lax
from jax.experimental import pallas as pl
from jax.experimental.pallas import tpu as pltpu
from jax.sharding import PartitionSpec as P


def step_kernel(a_cols, b_cols, want, a_ref, b_ref, *refs):
    if len(refs) == 8:
        mine_in, theirs_in, mine_ref, theirs_ref, tick, place_ref, sel_ref, slot_of = refs
    else:
        mine_in = theirs_in = None
        mine_ref, theirs_ref, tick, place_ref, sel_ref, slot_of = refs
    width = a_ref.shape[1]
    seg = a_ref.shape[2]
    slots = seg // width
    rows = place_ref.shape[0]
    outs = want.shape[0] // rows
    lane = lax.broadcasted_iota(jnp.int32, (width, 2 * width), 1)
    zero = jnp.zeros((width, 2 * width), b_ref.dtype)
    tick[0] = jnp.int32(0)

    def fill(k, carry):
        for q in range(slots):
            grp = b_ref[k, :, (q // 2) * 2 * width:(q // 2 + 1) * 2 * width]
            swap = pltpu.roll(grp, width, 1)
            for i in range(2):
                src = grp if i == q % 2 else swap
                keep = lane < width if i == 0 else lane >= width
                place_ref[k, q, i] = jnp.where(keep, src, zero)
        for i in range(2):
            place_ref[k, slots, i] = zero
        return carry

    lax.fori_loop(0, rows, fill, 0)
    for n in range(rows * rows):
        slot_of[n] = jnp.int32(slots)
    for n in range(rows * slots):
        slot_of[(n // slots) * rows + b_cols[n]] = jnp.int32(n % slots)

    def one_row(r, sel_ref):
        for p in range(slots):
            k = a_cols[r * slots + p]
            for g in range(outs // 2):
                picks = []
                for i in range(2):
                    hit = slot_of[k * rows + want[r * outs + 2 * g + i]]
                    picks.append(place_ref[k, hit, i])
                sel_ref[p * width:(p + 1) * width, g * 2 * width:(g + 1) * 2 * width] = picks[0] + picks[1]
        prod = jnp.dot(a_ref[r], sel_ref[...], preferred_element_type=jnp.float32)
        half = prod.shape[1] // 2
        if mine_in is None:
            mine_ref[r] = prod[:, :half]
            theirs_ref[r] = prod[:, half:]
        else:
            mine_ref[r] = mine_in[r] + prod[:, :half]
            theirs_ref[r] = theirs_in[r] + prod[:, half:]

    group = sel_ref.shape[0]

    def some_rows(n, carry):
        for m in range(group):
            one_row(group * n + m, sel_ref.at[m])
        return carry

    lax.fori_loop(0, rows // group, some_rows, 0)


def one_step(mine, theirs, left, right, a_cols, b_cols, want):
    rows, width, seg = left.shape[0] - 1, left.shape[1], left.shape[2]
    outs = want.shape[0] // rows
    share = outs // 2 * width
    sums = [] if mine is None else [mine, theirs]
    smem = pl.BlockSpec(memory_space=pltpu.SMEM)
    vmem = pl.BlockSpec(memory_space=pltpu.VMEM)
    cost = pl.CostEstimate(
        flops=2 * rows * width * seg * outs * width,
        transcendentals=0,
        bytes_accessed=2 * (left.size + right.size) + 4 * (2 + len(sums)) * rows * width * share,
    )
    return pl.pallas_call(
        step_kernel,
        in_specs=[smem] * 3 + [vmem] * (2 + len(sums)),
        out_specs=[vmem, vmem, smem],
        scratch_shapes=[
            pltpu.VMEM((rows, seg // width + 1, 2, width, 2 * width), right.dtype),
            pltpu.VMEM((8 if rows % 8 == 0 else 1, seg, outs * width), right.dtype),
            pltpu.SMEM((rows * rows,), jnp.int32),
        ],
        out_shape=[jax.ShapeDtypeStruct((rows, width, share), jnp.float32)] * 2
        + [jax.ShapeDtypeStruct((1,), jnp.int32)],
        input_output_aliases={5: 0, 6: 1} if sums else {},
        cost_estimate=cost,
    )(a_cols, b_cols, want, left, right, *sums)


def per_device(x_blocks, x_cols, x_count, out_cols):
    row_count, width, _, lanes = x_blocks.shape
    slots = lanes // width
    values = x_blocks[:, :, 0, :]
    slot_of_lane = lax.broadcasted_iota(jnp.int32, (1, 1, lanes), 2) // width
    values = jnp.where(slot_of_lane < x_count[:, :, None], values, jnp.zeros((), values.dtype))
    columns = x_cols[:, 0, :].reshape(-1)
    extra = jnp.zeros((1, width, lanes), values.dtype)
    extra = extra.at[0, 0, :columns.shape[0]].set(columns.astype(values.dtype))
    payload = jnp.concatenate([values, extra], axis=0)

    rows_n = lax.axis_size("row")
    cols_n = lax.axis_size("col")
    layers = lax.axis_size("layer")
    steps = rows_n // layers
    me_r = lax.axis_index("row")
    me_c = lax.axis_index("col")
    me_l = lax.axis_index("layer")

    def flat(r, c, l):
        return (r * cols_n + c) * layers + l

    outs = out_cols.shape[2]
    share = outs // layers
    both = jnp.concatenate([out_cols[:, 0, :], out_cols[:, 0, :]], axis=1)
    want = lax.dynamic_slice_in_dim(both, me_l * share, outs, axis=1).reshape(-1)
    mine = theirs = None
    tick = jnp.zeros((1,), jnp.int32)
    for s in range(steps):
        left_pairs = []
        right_pairs = []
        for r in range(rows_n):
            for c in range(cols_n):
                for l in range(layers):
                    t = r ^ c ^ (s + l * steps)
                    left_pairs.append((flat(t, c, l), flat(r, c, l)))
                    right_pairs.append((flat(r, t, l), flat(r, c, l)))
        left = lax.ppermute(payload, ("row", "col", "layer"), left_pairs)
        right = lax.ppermute(payload, ("row", "col", "layer"), right_pairs)
        n = columns.shape[0]
        a_cols = left[row_count, 0, :n].astype(jnp.int32) + tick
        b_cols = right[row_count, 0, :n].astype(jnp.int32) + tick
        mine, theirs, tick = one_step(mine, theirs, left, right, a_cols, b_cols, want)

    got = lax.ppermute(theirs, "layer", [(0, 1), (1, 0)])
    return mine[:, :, None, :] + got[:, :, None, :]


def solution(mesh):
    placed = (
        P("col", None, "row", None),
        P("col", "row", None),
        P("col", "row"),
        P("col", "row", None),
    )
    return jax.shard_map(
        per_device,
        mesh=mesh,
        in_specs=placed,
        out_specs=P("col", None, "row", "layer"),
        check_vma=False,
    )
```

```python
import functools

import jax
import jax.numpy as jnp
from jax import lax
from jax.experimental import pallas as pl
from jax.experimental.pallas import tpu as pltpu
from jax.sharding import PartitionSpec as P


def step_kernel(width, a_cols, b_cols, want, a_ref, b_ref, *refs):
    if len(refs) == 8:
        mine_in, theirs_in, mine_ref, theirs_ref, tick, place_ref, sel_ref, slot_of = refs
    else:
        mine_in = theirs_in = None
        mine_ref, theirs_ref, tick, place_ref, sel_ref, slot_of = refs
    seg = a_ref.shape[1]
    slots = seg // width
    rows = place_ref.shape[0]
    outs = want.shape[0] // rows
    lane = lax.broadcasted_iota(jnp.int32, (width, 2 * width), 1)
    zero = jnp.zeros((width, 2 * width), b_ref.dtype)
    tick[0] = jnp.int32(0)

    def fill(k, carry):
        for q in range(slots):
            grp = b_ref[pl.ds(pl.multiple_of(k * width, width), width), (q // 2) * 2 * width:(q // 2 + 1) * 2 * width]
            swap = pltpu.roll(grp, width, 1)
            for i in range(2):
                src = grp if i == q % 2 else swap
                keep = lane < width if i == 0 else lane >= width
                place_ref[k, q, i] = jnp.where(keep, src, zero)
        for i in range(2):
            place_ref[k, slots, i] = zero
        return carry

    lax.fori_loop(0, rows, fill, 0)
    for n in range(rows * rows):
        slot_of[n] = jnp.int32(slots)
    for n in range(rows * slots):
        slot_of[(n // slots) * rows + b_cols[n]] = jnp.int32(n % slots)

    def one_row(r, sel_ref):
        for p in range(slots):
            k = a_cols[r * slots + p]
            for g in range(outs // 2):
                picks = []
                for i in range(2):
                    hit = slot_of[k * rows + want[r * outs + 2 * g + i]]
                    picks.append(place_ref[k, hit, i])
                sel_ref[p * width:(p + 1) * width, g * 2 * width:(g + 1) * 2 * width] = picks[0] + picks[1]
        left_rows = a_ref[pl.ds(pl.multiple_of(r * width, width), width), :]
        prod = jnp.dot(left_rows, sel_ref[...], preferred_element_type=jnp.float32)
        half = prod.shape[1] // 2
        if mine_in is None:
            mine_ref[r] = prod[:, :half]
            theirs_ref[r] = prod[:, half:]
        else:
            mine_ref[r] = mine_in[r] + prod[:, :half]
            theirs_ref[r] = theirs_in[r] + prod[:, half:]

    group = sel_ref.shape[0]

    def some_rows(n, carry):
        for m in range(group):
            one_row(group * n + m, sel_ref.at[m])
        return carry

    lax.fori_loop(0, rows // group, some_rows, 0)


def one_step(mine, theirs, left, right, a_cols, b_cols, want, width):
    rows, seg = left.shape[0] // width, left.shape[1]
    outs = want.shape[0] // rows
    share = outs // 2 * width
    sums = [] if mine is None else [mine, theirs]
    smem = pl.BlockSpec(memory_space=pltpu.SMEM)
    vmem = pl.BlockSpec(memory_space=pltpu.VMEM)
    cost = pl.CostEstimate(
        flops=2 * rows * width * seg * outs * width,
        transcendentals=0,
        bytes_accessed=2 * (left.size + right.size) + 4 * (2 + len(sums)) * rows * width * share,
    )
    return pl.pallas_call(
        functools.partial(step_kernel, width),
        in_specs=[smem] * 3 + [vmem] * (2 + len(sums)),
        out_specs=[vmem, vmem, smem],
        scratch_shapes=[
            pltpu.VMEM((rows, seg // width + 1, 2, width, 2 * width), right.dtype),
            pltpu.VMEM((8 if rows % 8 == 0 else 1, seg, outs * width), right.dtype),
            pltpu.SMEM((rows * rows,), jnp.int32),
        ],
        out_shape=[jax.ShapeDtypeStruct((rows, width, share), jnp.float32)] * 2
        + [jax.ShapeDtypeStruct((1,), jnp.int32)],
        input_output_aliases={5: 0, 6: 1} if sums else {},
        cost_estimate=cost,
    )(a_cols, b_cols, want, left, right, *sums)


def per_device(x_blocks, x_cols, x_count, out_cols):
    row_count, width, _, lanes = x_blocks.shape
    slots = lanes // width
    values = x_blocks[:, :, 0, :]
    slot_of_lane = lax.broadcasted_iota(jnp.int32, (1, 1, lanes), 2) // width
    values = jnp.where(slot_of_lane < x_count[:, :, None], values, jnp.zeros((), values.dtype))
    columns = x_cols[:, 0, :].reshape(-1)
    pad = 16
    extra = jnp.zeros((pad, lanes), values.dtype)
    extra = extra.at[0, :columns.shape[0]].set(columns.astype(values.dtype))
    payload = jnp.concatenate([values.reshape(row_count * width, lanes), extra], axis=0)

    rows_n = lax.axis_size("row")
    cols_n = lax.axis_size("col")
    layers = lax.axis_size("layer")
    steps = rows_n // layers
    me_r = lax.axis_index("row")
    me_c = lax.axis_index("col")
    me_l = lax.axis_index("layer")

    def flat(r, c, l):
        return (r * cols_n + c) * layers + l

    outs = out_cols.shape[2]
    share = outs // layers
    both = jnp.concatenate([out_cols[:, 0, :], out_cols[:, 0, :]], axis=1)
    want = lax.dynamic_slice_in_dim(both, me_l * share, outs, axis=1).reshape(-1)
    mine = theirs = None
    tick = jnp.zeros((1,), jnp.int32)
    for s in range(steps):
        left_pairs = []
        right_pairs = []
        for r in range(rows_n):
            for c in range(cols_n):
                for l in range(layers):
                    t = r ^ c ^ (s + l * steps)
                    left_pairs.append((flat(t, c, l), flat(r, c, l)))
                    right_pairs.append((flat(r, t, l), flat(r, c, l)))
        left = lax.ppermute(payload, ("row", "col", "layer"), left_pairs)
        right = lax.ppermute(payload, ("row", "col", "layer"), right_pairs)
        n = columns.shape[0]
        a_cols = left[row_count * width, :n].astype(jnp.int32) + tick
        b_cols = right[row_count * width, :n].astype(jnp.int32) + tick
        mine, theirs, tick = one_step(mine, theirs, left, right, a_cols, b_cols, want, width)

    got = lax.ppermute(theirs, "layer", [(0, 1), (1, 0)])
    return mine[:, :, None, :] + got[:, :, None, :]


def solution(mesh):
    placed = (
        P("col", None, "row", None),
        P("col", "row", None),
        P("col", "row"),
        P("col", "row", None),
    )
    return jax.shard_map(
        per_device,
        mesh=mesh,
        in_specs=placed,
        out_specs=P("col", None, "row", "layer"),
        check_vma=False,
    )
```

```python
import functools

import jax
import jax.numpy as jnp
from jax import lax
from jax.experimental import pallas as pl
from jax.experimental.pallas import tpu as pltpu
from jax.sharding import PartitionSpec as P


def step_kernel(width, a_cols, b_cols, want, a_ref, b_ref, *refs):
    if len(refs) == 8:
        mine_in, theirs_in, mine_ref, theirs_ref, tick, place_ref, sel_ref, slot_of = refs
    else:
        mine_in = theirs_in = None
        mine_ref, theirs_ref, tick, place_ref, sel_ref, slot_of = refs
    seg = a_ref.shape[1]
    slots = seg // width
    rows = place_ref.shape[0]
    outs = want.shape[0] // rows
    lane = lax.broadcasted_iota(jnp.int32, (width, 2 * width), 1)
    zero = jnp.zeros((width, 2 * width), b_ref.dtype)
    tick[0] = jnp.int32(0)

    def fill(k, carry):
        for q in range(slots):
            grp = b_ref[pl.ds(pl.multiple_of(k * width, width), width), (q // 2) * 2 * width:(q // 2 + 1) * 2 * width]
            swap = pltpu.roll(grp, width, 1)
            for i in range(2):
                src = grp if i == q % 2 else swap
                keep = lane < width if i == 0 else lane >= width
                place_ref[k, q, i] = jnp.where(keep, src, zero)
        for i in range(2):
            place_ref[k, slots, i] = zero
        return carry

    lax.fori_loop(0, rows, fill, 0, unroll=True)
    for n in range(rows * rows):
        slot_of[n] = jnp.int32(slots)
    for n in range(rows * slots):
        slot_of[(n // slots) * rows + b_cols[n]] = jnp.int32(n % slots)

    def one_row(r, sel_ref):
        for p in range(slots):
            k = a_cols[r * slots + p]
            for g in range(outs // 2):
                picks = []
                for i in range(2):
                    hit = slot_of[k * rows + want[r * outs + 2 * g + i]]
                    picks.append(place_ref[k, hit, i])
                sel_ref[p * width:(p + 1) * width, g * 2 * width:(g + 1) * 2 * width] = picks[0] + picks[1]
        left_rows = a_ref[pl.ds(pl.multiple_of(r * width, width), width), :]
        prod = jnp.dot(left_rows, sel_ref[...], preferred_element_type=jnp.float32)
        half = prod.shape[1] // 2
        if mine_in is None:
            mine_ref[r] = prod[:, :half]
            theirs_ref[r] = prod[:, half:]
        else:
            mine_ref[r] = mine_in[r] + prod[:, :half]
            theirs_ref[r] = theirs_in[r] + prod[:, half:]

    group = sel_ref.shape[0]

    def some_rows(n, carry):
        for m in range(group):
            one_row(group * n + m, sel_ref.at[m])
        return carry

    lax.fori_loop(0, rows // group, some_rows, 0)


def one_step(mine, theirs, left, right, a_cols, b_cols, want, width):
    rows, seg = left.shape[0] // width, left.shape[1]
    outs = want.shape[0] // rows
    share = outs // 2 * width
    sums = [] if mine is None else [mine, theirs]
    smem = pl.BlockSpec(memory_space=pltpu.SMEM)
    vmem = pl.BlockSpec(memory_space=pltpu.VMEM)
    cost = pl.CostEstimate(
        flops=2 * rows * width * seg * outs * width,
        transcendentals=0,
        bytes_accessed=2 * (left.size + right.size) + 4 * (2 + len(sums)) * rows * width * share,
    )
    return pl.pallas_call(
        functools.partial(step_kernel, width),
        in_specs=[smem] * 3 + [vmem] * (2 + len(sums)),
        out_specs=[vmem, vmem, smem],
        scratch_shapes=[
            pltpu.VMEM((rows, seg // width + 1, 2, width, 2 * width), right.dtype),
            pltpu.VMEM((8 if rows % 8 == 0 else 1, seg, outs * width), right.dtype),
            pltpu.SMEM((rows * rows,), jnp.int32),
        ],
        out_shape=[jax.ShapeDtypeStruct((rows, width, share), jnp.float32)] * 2
        + [jax.ShapeDtypeStruct((1,), jnp.int32)],
        input_output_aliases={5: 0, 6: 1} if sums else {},
        cost_estimate=cost,
    )(a_cols, b_cols, want, left, right, *sums)


def per_device(x_blocks, x_cols, x_count, out_cols):
    row_count, width, _, lanes = x_blocks.shape
    slots = lanes // width
    values = x_blocks[:, :, 0, :]
    slot_of_lane = lax.broadcasted_iota(jnp.int32, (1, 1, lanes), 2) // width
    values = jnp.where(slot_of_lane < x_count[:, :, None], values, jnp.zeros((), values.dtype))
    columns = x_cols[:, 0, :].reshape(-1)
    pad = 16
    extra = jnp.zeros((pad, lanes), values.dtype)
    extra = extra.at[0, :columns.shape[0]].set(columns.astype(values.dtype))
    payload = jnp.concatenate([values.reshape(row_count * width, lanes), extra], axis=0)

    rows_n = lax.axis_size("row")
    cols_n = lax.axis_size("col")
    layers = lax.axis_size("layer")
    steps = rows_n // layers
    me_r = lax.axis_index("row")
    me_c = lax.axis_index("col")
    me_l = lax.axis_index("layer")

    def flat(r, c, l):
        return (r * cols_n + c) * layers + l

    outs = out_cols.shape[2]
    share = outs // layers
    both = jnp.concatenate([out_cols[:, 0, :], out_cols[:, 0, :]], axis=1)
    want = lax.dynamic_slice_in_dim(both, me_l * share, outs, axis=1).reshape(-1)
    mine = theirs = None
    tick = jnp.zeros((1,), jnp.int32)
    for s in range(steps):
        left_pairs = []
        right_pairs = []
        for r in range(rows_n):
            for c in range(cols_n):
                for l in range(layers):
                    t = r ^ c ^ (s + l * steps)
                    left_pairs.append((flat(t, c, l), flat(r, c, l)))
                    right_pairs.append((flat(r, t, l), flat(r, c, l)))
        left = lax.ppermute(payload, ("row", "col", "layer"), left_pairs)
        right = lax.ppermute(payload, ("row", "col", "layer"), right_pairs)
        n = columns.shape[0]
        a_cols = left[row_count * width, :n].astype(jnp.int32) + tick
        b_cols = right[row_count * width, :n].astype(jnp.int32) + tick
        mine, theirs, tick = one_step(mine, theirs, left, right, a_cols, b_cols, want, width)

    got = lax.ppermute(theirs, "layer", [(0, 1), (1, 0)])
    return mine[:, :, None, :] + got[:, :, None, :]


def solution(mesh):
    placed = (
        P("col", None, "row", None),
        P("col", "row", None),
        P("col", "row"),
        P("col", "row", None),
    )
    return jax.shard_map(
        per_device,
        mesh=mesh,
        in_specs=placed,
        out_specs=P("col", None, "row", "layer"),
        check_vma=False,
    )
```

```python
import functools

import jax
import jax.numpy as jnp
from jax import lax
from jax.experimental import pallas as pl
from jax.experimental.pallas import tpu as pltpu
from jax.sharding import PartitionSpec as P


def step_kernel(width, a_cols, b_cols, want, a_ref, b_ref, *refs):
    if len(refs) == 8:
        mine_in, theirs_in, mine_ref, theirs_ref, tick, place_ref, sel_ref, slot_of = refs
    else:
        mine_in = theirs_in = None
        mine_ref, theirs_ref, tick, place_ref, sel_ref, slot_of = refs
    seg = a_ref.shape[1]
    slots = seg // width
    rows = place_ref.shape[0]
    outs = want.shape[0] // rows
    lane = lax.broadcasted_iota(jnp.int32, (width, 2 * width), 1)
    zero = jnp.zeros((width, 2 * width), b_ref.dtype)
    tick[0] = jnp.int32(0)

    def fill(k, carry):
        for q in range(slots):
            grp = b_ref[pl.ds(pl.multiple_of(k * width, width), width), (q // 2) * 2 * width:(q // 2 + 1) * 2 * width]
            swap = pltpu.roll(grp, width, 1)
            for i in range(2):
                src = grp if i == q % 2 else swap
                keep = lane < width if i == 0 else lane >= width
                place_ref[k, q, i] = jnp.where(keep, src, zero)
        for i in range(2):
            place_ref[k, slots, i] = zero
        return carry

    lax.fori_loop(0, rows, fill, 0, unroll=True)
    for n in range(rows * rows):
        slot_of[n] = jnp.int32(slots)
    for n in range(rows * slots):
        slot_of[(n // slots) * rows + b_cols[n]] = jnp.int32(n % slots)

    def one_row(r, sel_ref):
        for p in range(slots):
            k = a_cols[r * slots + p]
            for g in range(outs // 2):
                picks = []
                for i in range(2):
                    hit = slot_of[k * rows + want[r * outs + 2 * g + i]]
                    picks.append(place_ref[k, hit, i])
                sel_ref[p * width:(p + 1) * width, g * 2 * width:(g + 1) * 2 * width] = picks[0] + picks[1]
        left_rows = a_ref[pl.ds(pl.multiple_of(r * width, width), width), :]
        prod = jnp.dot(left_rows, sel_ref[...], preferred_element_type=jnp.float32)
        half = prod.shape[1] // 2
        if mine_in is None:
            mine_ref[r] = prod[:, :half]
            theirs_ref[r] = prod[:, half:]
        else:
            mine_ref[r] = mine_in[r] + prod[:, :half]
            theirs_ref[r] = theirs_in[r] + prod[:, half:]

    group = sel_ref.shape[0]

    def some_rows(n, carry):
        for m in range(group):
            one_row(group * n + m, sel_ref.at[m])
        return carry

    lax.fori_loop(0, rows // group, some_rows, 0, unroll=True)


def one_step(mine, theirs, left, right, a_cols, b_cols, want, width):
    rows, seg = left.shape[0] // width, left.shape[1]
    outs = want.shape[0] // rows
    share = outs // 2 * width
    sums = [] if mine is None else [mine, theirs]
    smem = pl.BlockSpec(memory_space=pltpu.SMEM)
    vmem = pl.BlockSpec(memory_space=pltpu.VMEM)
    cost = pl.CostEstimate(
        flops=2 * rows * width * seg * outs * width,
        transcendentals=0,
        bytes_accessed=2 * (left.size + right.size) + 4 * (2 + len(sums)) * rows * width * share,
    )
    return pl.pallas_call(
        functools.partial(step_kernel, width),
        in_specs=[smem] * 3 + [vmem] * (2 + len(sums)),
        out_specs=[vmem, vmem, smem],
        scratch_shapes=[
            pltpu.VMEM((rows, seg // width + 1, 2, width, 2 * width), right.dtype),
            pltpu.VMEM((16 if rows % 16 == 0 else 1, seg, outs * width), right.dtype),
            pltpu.SMEM((rows * rows,), jnp.int32),
        ],
        out_shape=[jax.ShapeDtypeStruct((rows, width, share), jnp.float32)] * 2
        + [jax.ShapeDtypeStruct((1,), jnp.int32)],
        input_output_aliases={5: 0, 6: 1} if sums else {},
        cost_estimate=cost,
    )(a_cols, b_cols, want, left, right, *sums)


def per_device(x_blocks, x_cols, x_count, out_cols):
    row_count, width, _, lanes = x_blocks.shape
    slots = lanes // width
    values = x_blocks[:, :, 0, :]
    slot_of_lane = lax.broadcasted_iota(jnp.int32, (1, 1, lanes), 2) // width
    values = jnp.where(slot_of_lane < x_count[:, :, None], values, jnp.zeros((), values.dtype))
    columns = x_cols[:, 0, :].reshape(-1)
    pad = 16
    extra = jnp.zeros((pad, lanes), values.dtype)
    extra = extra.at[0, :columns.shape[0]].set(columns.astype(values.dtype))
    payload = jnp.concatenate([values.reshape(row_count * width, lanes), extra], axis=0)

    rows_n = lax.axis_size("row")
    cols_n = lax.axis_size("col")
    layers = lax.axis_size("layer")
    steps = rows_n // layers
    me_r = lax.axis_index("row")
    me_c = lax.axis_index("col")
    me_l = lax.axis_index("layer")

    def flat(r, c, l):
        return (r * cols_n + c) * layers + l

    outs = out_cols.shape[2]
    share = outs // layers
    both = jnp.concatenate([out_cols[:, 0, :], out_cols[:, 0, :]], axis=1)
    want = lax.dynamic_slice_in_dim(both, me_l * share, outs, axis=1).reshape(-1)
    mine = theirs = None
    tick = jnp.zeros((1,), jnp.int32)
    for s in range(steps):
        left_pairs = []
        right_pairs = []
        for r in range(rows_n):
            for c in range(cols_n):
                for l in range(layers):
                    t = r ^ c ^ (s + l * steps)
                    left_pairs.append((flat(t, c, l), flat(r, c, l)))
                    right_pairs.append((flat(r, t, l), flat(r, c, l)))
        left = lax.ppermute(payload, ("row", "col", "layer"), left_pairs)
        right = lax.ppermute(payload, ("row", "col", "layer"), right_pairs)
        n = columns.shape[0]
        a_cols = left[row_count * width, :n].astype(jnp.int32)
        b_cols = right[row_count * width, :n].astype(jnp.int32) + tick
        mine, theirs, tick = one_step(mine, theirs, left, right, a_cols, b_cols, want, width)

    got = lax.ppermute(theirs, "layer", [(0, 1), (1, 0)])
    return mine[:, :, None, :] + got[:, :, None, :]


def solution(mesh):
    placed = (
        P("col", None, "row", None),
        P("col", "row", None),
        P("col", "row"),
        P("col", "row", None),
    )
    return jax.shard_map(
        per_device,
        mesh=mesh,
        in_specs=placed,
        out_specs=P("col", None, "row", "layer"),
        check_vma=False,
    )
```
